128 devices in a mesh: group: 4 (over x_hi, core), tp: 32 (over z, y, x_lo).
Axes of the slice: x: 4 (x_hi: 2, x_lo: 2; x = x_hi * 2 + x_lo), y: 4, z: 4, core: 2. Of those that a mesh axis runs over, the one named last changes fastest.
Arguments:
- hidden: bfloat16 [4096, 28672], P('group', 'tp'), may hold values from -6 to 6
- residual: bfloat16 [4096, 8192], P('group', 'tp'), may hold values from -6 to 6
- down_projection_weight: bfloat16 [28672, 8192], P('tp'), may hold values from -0.03125 to 0.03125
- adapter_down_maps: bfloat16 [128, 64, 28672], P('group', None, 'tp'), may hold values from -0.03125 to 0.03125
- adapter_up_maps: bfloat16 [128, 64, 8192], P('group', None, 'tp'), may hold values from -0.75 to 0.75
- row_adapter_index: int32 [4096, 1], P('group'), may hold values from 0 to 127; in each aligned block of 1024 rows (0 to 1023, 1024 to 2047, ...) at most 16 rows name the same one
Outputs:
- layer_out: bfloat16 [4096, 8192], P('group', 'tp')
The draws below stay inside these ranges and needn't reach their ends.
Inputs may be any that keep to these rules, and one draw needn't show every extreme that they name: `row_adapter_index`: within the 1024 rows of one group no adapter is named by more than 16 rows; in some group some adapter is named by exactly 16 rows; every adapter is named by some row.
All inputs are finite; a program needn't handle non-finite values.
Results may differ from the reference program's by a relative error of at most 0.02.
Values may be sent and summed in bfloat16 or wider, within the bound.
No kernel may reach another device: no remote copies, remote signals or barrier semaphores. Data moves between devices by JAX's collectives and lax.ppermute only.
A program may use at most 128 MiB of HBM per device.

```python
import math
import jax
import jax.numpy as jnp
import numpy as np
from jax import lax

MODEL_WIDTH = 8192
HIDDEN_UNITS = 28672
ADAPTER_RANK = 64
MOST = 16
ROWS_G = 1024
ROWS = 4096
ADAPTER_COUNT = 128
N_TP = 32


def levels(stream_key, shape, cuts, least, top_value):
    def one(dim, parts):
        heights = jax.random.uniform(jax.random.fold_in(jax.random.fold_in(stream_key, 6), dim), (parts,), jnp.float32, least / len(cuts), top_value / len(cuts))
        return jnp.repeat(jnp.exp(heights), shape[dim] // parts).reshape((-1,) + (1,) * (len(shape) - dim - 1))

    gain = one(*cuts[0])
    for cut in cuts[1:]:
        gain = gain * one(*cut)
    return gain


def shared_out(stream_key, own, number, rows, number_of, top, most, slope):
    order = jax.random.permutation(stream_key, number_of)
    crowded, ordinary = portions_of(number_of, rows * top, most, slope, True), portions_of(number_of, rows * top, most, slope, False)
    places = jnp.arange(number_of)

    def named(tallies, turn):
        used = int((tallies > 0).sum())
        fixed = max(1, used // 4)
        moved = fixed + (places - fixed + turn * (used - fixed)) % max(1, number_of - fixed)
        return jnp.zeros((number_of,), jnp.int32).at[order[jnp.where(places < fixed, places, moved)]].set(jnp.asarray(tallies, jnp.int32))

    tallies = jnp.where(number % 4 == 0, named(crowded, number // 4), named(ordinary, number - number // 4 - 1))
    mixed = jax.random.permutation(jax.random.fold_in(own, 3), number_of)
    source_of, taker = mixed[0:number_of // 2 * 2:2], mixed[1:number_of // 2 * 2:2]
    room = jnp.minimum(tallies[source_of] - 1, most - tallies[taker]) // 2
    room = jnp.where((source_of == order[0]) | (taker == order[0]) | (tallies[taker] == 0), 0, jnp.maximum(room, 0))
    moved = jax.random.randint(jax.random.fold_in(own, 4), (number_of // 2,), 0, 1 << 20) % (room + 1)
    tallies = tallies.at[source_of].add(-moved).at[taker].add(moved)
    items = jnp.searchsorted(jnp.cumsum(tallies), jnp.arange(rows * top), side="right").astype(jnp.int32)
    listing = items.reshape(top, rows).T
    listing = listing[jax.random.permutation(jax.random.fold_in(own, 1), rows)]
    turn = jax.random.randint(jax.random.fold_in(own, 2), (rows, 1), 0, top)
    return jnp.take_along_axis(listing, (jnp.arange(top)[None, :] + turn) % top, axis=1)


def portions_of(count, total, reach, slope, full):
    loads = [(1 << 20) // math.isqrt(grade ** slope) + 1 for grade in range(1, count + 1)]
    largest = reach if full else min(reach, max(-(-total // count), total * loads[0] // sum(loads)))
    least = 1 if total - largest >= count - 1 else 0
    holding, spare = [largest] + [least] * (count - 1), total - largest - least * (count - 1)
    while spare > 0:
        candidates = [i for i in range(1, count) if holding[i] < largest] or [i for i in range(1, count) if holding[i] < reach]
        mass, left = sum([loads[i] for i in candidates]), spare
        for i in candidates:
            more = min(reach - holding[i], max(1, left * loads[i] // mass), spare)
            holding[i] = holding[i] + more
            spare = spare - more
    return np.array(holding)


def noise(key, dims, scale, most, pieces=(), kind=jnp.bfloat16):
    drawn = scale * jax.random.normal(key, dims, jnp.float32)
    if pieces:
        drawn = drawn * levels(key, dims, pieces, -0.22, 0.18)
    return jnp.clip(drawn, -most, most).astype(kind)


def setup_inputs(seed: int = 0) -> dict:
    streams_of = jax.random.split(jax.random.key(seed), 7)
    hidden = noise(streams_of[0], (ROWS, HIDDEN_UNITS), 1.0, 6.0, ((0, 4), (1, 32)))
    residual = noise(streams_of[1], (ROWS, MODEL_WIDTH), 1.0, 6.0, ((0, 4), (1, 32)))
    down_projection_weight = noise(streams_of[2], (HIDDEN_UNITS, MODEL_WIDTH), HIDDEN_UNITS ** -0.5, 0.03125, ((0, 32),))
    adapter_down_maps = noise(streams_of[3], (ADAPTER_COUNT, ADAPTER_RANK, HIDDEN_UNITS), HIDDEN_UNITS ** -0.5, 0.03125, ((0, 4), (2, 32)))
    adapter_up_maps = noise(streams_of[4], (ADAPTER_COUNT, ADAPTER_RANK, MODEL_WIDTH), ADAPTER_RANK ** -0.5, 0.75, ((0, 4), (2, 32)))
    row_adapter_index_keys = jax.random.split(jax.random.fold_in(streams_of[5], 1), ROWS // ROWS_G)
    row_adapter_index_turns = jax.random.permutation(jax.random.fold_in(streams_of[5], 3), ROWS // ROWS_G)
    row_adapter_index = jax.vmap(lambda own, number: shared_out(jax.random.fold_in(streams_of[5], 2), own, number, ROWS_G, ADAPTER_COUNT, 1, MOST, 2))(row_adapter_index_keys, row_adapter_index_turns).reshape((ROWS, 1))
    return dict(hidden=hidden, residual=residual, down_projection_weight=down_projection_weight, adapter_down_maps=adapter_down_maps, adapter_up_maps=adapter_up_maps, row_adapter_index=row_adapter_index)


def reference(hidden, residual, down_projection_weight, adapter_down_maps, adapter_up_maps, row_adapter_index):
    piece = HIDDEN_UNITS // N_TP

    def add_piece(total, index):
        start = index * piece
        part_hidden = lax.dynamic_slice_in_dim(hidden, start, piece, 1)
        part_weight = lax.dynamic_slice_in_dim(down_projection_weight, start, piece, 0)
        term = jnp.dot(part_hidden, part_weight, preferred_element_type=jnp.float32).astype(jnp.bfloat16)
        term = lax.optimization_barrier(term)
        return total + term.astype(jnp.float32), None

    base, _ = lax.scan(add_piece, jnp.zeros((ROWS, MODEL_WIDTH), jnp.float32), jnp.arange(N_TP, dtype=jnp.int32))

    def one_row(item):
        decode_row_vector, adapter_index = item
        rank_mixture = jnp.dot(adapter_down_maps[adapter_index], decode_row_vector, preferred_element_type=jnp.float32).astype(jnp.bfloat16)
        return jnp.dot(rank_mixture, adapter_up_maps[adapter_index], preferred_element_type=jnp.float32).astype(jnp.bfloat16)

    delta = lax.map(one_row, (hidden, row_adapter_index[:, 0]))
    total = residual.astype(jnp.float32) + base + delta.astype(jnp.float32)
    return total.astype(jnp.bfloat16)
```

```python
import jax
import jax.numpy as jnp
from jax import lax
from jax.sharding import Mesh
from jax.sharding import PartitionSpec as P

MOST = 16
GROUP = ("xh", "c")
TP = ("z", "y", "xl")


def _blk(blocks, k):
    return lax.dynamic_index_in_dim(blocks, k, 0, keepdims=False)


def ring_rs(x, axis, n, out_f32=False):
    i = lax.axis_index(axis)
    if n == 2:
        recv = lax.ppermute(_blk(x, 1 - i), axis, [(0, 1), (1, 0)])
        total = recv.astype(jnp.float32) + _blk(x, i).astype(jnp.float32)
        return total if out_f32 else total.astype(jnp.bfloat16)
    h = x.shape[-1] // 2
    xa, xb = x[..., :h], x[..., h:]
    acc_a = _blk(xa, (i - 1) % n)
    acc_b = _blk(xb, (i + 1) % n)
    fw = [(j, (j + 1) % n) for j in range(n)]
    bw = [(j, (j - 1) % n) for j in range(n)]
    for s in range(n - 1):
        ra = lax.ppermute(acc_a, axis, fw)
        rb = lax.ppermute(acc_b, axis, bw)
        fa = ra.astype(jnp.float32) + _blk(xa, (i - 2 - s) % n).astype(jnp.float32)
        fb = rb.astype(jnp.float32) + _blk(xb, (i + 2 + s) % n).astype(jnp.float32)
        last = s == n - 2
        acc_a = fa if (last and out_f32) else fa.astype(jnp.bfloat16)
        acc_b = fb if (last and out_f32) else fb.astype(jnp.bfloat16)
    return jnp.concatenate([acc_a, acc_b], axis=-1)


def all_reduce_axis(x, axis, n):
    total = x
    for d in range(1, n):
        total = total + lax.ppermute(x, axis, [(j, (j + d) % n) for j in range(n)])
    return total


def per_device(
    hidden, residual, down_projection_weight, adapter_down_maps, adapter_up_maps, row_adapter_index
):
    group_count = 4
    rows, hidden_cols = hidden.shape
    resident_adapters = adapter_down_maps.shape[0]
    adapter_total = resident_adapters * group_count
    per_owner = resident_adapters * MOST
    g = lax.axis_index(GROUP)

    row_adapter = row_adapter_index[:, 0]
    one_hot = (row_adapter[:, None] == jnp.arange(adapter_total, dtype=jnp.int32)[None, :]).astype(
        jnp.int32
    )
    before = jnp.cumsum(one_hot, axis=0) - 1
    slot_rank = jnp.sum(one_hot * before, axis=1)
    slot_index = row_adapter * MOST + slot_rank
    parcels = jnp.zeros((adapter_total * MOST, hidden_cols), jnp.bfloat16).at[slot_index].set(hidden)
    parcels = parcels.reshape(group_count, per_owner, hidden_cols)

    shifted = [_blk(parcels, g)]
    for d in range(1, group_count):
        perm = [(j, (j + d) % group_count) for j in range(group_count)]
        shifted.append(lax.ppermute(_blk(parcels, (g + d) % group_count), GROUP, perm))
    mine = jnp.stack(shifted).reshape(group_count, resident_adapters, MOST, hidden_cols)

    half = rows // 2
    w = down_projection_weight
    feature_blocks = (4, 4, 2, w.shape[1] // 32)

    def partial(h):
        out = lax.dot_general(w, h, (((0,), (1,)), ((), ())), preferred_element_type=jnp.float32)
        return out.astype(jnp.bfloat16).reshape(*feature_blocks, h.shape[0])

    part_a = partial(hidden[:half])
    part_b = partial(hidden[half:])

    partial_mix = jnp.einsum(
        "dlmf,lrf->dlmr", mine, adapter_down_maps, preferred_element_type=jnp.float32
    )

    red_a = ring_rs(part_a, "z", 4)
    red_b = ring_rs(jnp.swapaxes(part_b, 0, 1), "y", 4)
    red_a = ring_rs(red_a, "y", 4)
    red_b = ring_rs(red_b, "z", 4)
    base_cols = ring_rs(jnp.concatenate([red_a, red_b], axis=-1), "xl", 2, out_f32=True)

    mix = partial_mix
    for axis, n in (("z", 4), ("y", 4), ("xl", 2)):
        mix = all_reduce_axis(mix, axis, n)
    rank_mix = mix.astype(jnp.bfloat16)
    delta_mine = jnp.einsum(
        "dlmr,lrc->dlmc", rank_mix, adapter_up_maps, preferred_element_type=jnp.float32
    ).astype(jnp.bfloat16)
    feature_cols = delta_mine.shape[-1]
    delta_mine = delta_mine.reshape(group_count, per_owner, feature_cols)

    back = [delta_mine[0]]
    for d in range(1, group_count):
        perm = [(j, (j - d) % group_count) for j in range(group_count)]
        back.append(lax.ppermute(delta_mine[d], GROUP, perm))
    back = jnp.stack(back).reshape(group_count * per_owner, feature_cols)
    owner = slot_index // per_owner
    place = ((owner - g) % group_count) * per_owner + slot_index % per_owner
    delta_rows = back[place]

    total = residual.astype(jnp.float32) + base_cols.T + delta_rows.astype(jnp.float32)
    return total.astype(jnp.bfloat16)


def solution(mesh):
    fine = Mesh(mesh.devices.reshape(2, 2, 4, 4, 2), GROUP + TP)
    in_specs = (
        P(GROUP, TP),
        P(GROUP, TP),
        P(TP, None),
        P(GROUP, None, TP),
        P(GROUP, None, TP),
        P(GROUP, None),
    )
    out_specs = P(GROUP, TP)
    return jax.shard_map(
        per_device, mesh=fine, in_specs=in_specs, out_specs=out_specs, check_vma=False
    )
```

```python
import jax
import jax.numpy as jnp
from jax import lax
from jax.sharding import Mesh
from jax.sharding import PartitionSpec as P

MOST = 16
GROUP = ("xh", "c")
TP = ("z", "y", "xl")


def _pick(x, k, dim):
    return lax.dynamic_index_in_dim(x, k, dim, keepdims=False)


def reduce_scatter_axis(x, axis, n, dim, out_f32=False):
    i = lax.axis_index(axis)
    f32 = jnp.float32
    if n == 2:
        recv = lax.ppermute(_pick(x, 1 - i, dim), axis, [(0, 1), (1, 0)])
        total = recv.astype(f32) + _pick(x, i, dim).astype(f32)
        return total if out_f32 else total.astype(jnp.bfloat16)
    assert n == 4
    fw = [(j, (j + 1) % n) for j in range(n)]
    bw = [(j, (j - 1) % n) for j in range(n)]
    h = x.shape[-1] // 2
    far = _pick(x, (i + 2) % n, dim)
    got_a = lax.ppermute(far[..., :h], axis, fw)
    got_b = lax.ppermute(far[..., h:], axis, bw)
    nxt = _pick(x, (i + 1) % n, dim)
    prv = _pick(x, (i - 1) % n, dim)
    to_next = jnp.concatenate(
        [(nxt[..., :h].astype(f32) + got_a.astype(f32)).astype(jnp.bfloat16), nxt[..., h:]], axis=-1
    )
    to_prev = jnp.concatenate(
        [prv[..., :h], (prv[..., h:].astype(f32) + got_b.astype(f32)).astype(jnp.bfloat16)], axis=-1
    )
    from_prev = lax.ppermute(to_next, axis, fw)
    from_next = lax.ppermute(to_prev, axis, bw)
    total = from_prev.astype(f32) + from_next.astype(f32) + _pick(x, i, dim).astype(f32)
    return total if out_f32 else total.astype(jnp.bfloat16)


def all_reduce_axis(x, axis, n):
    total = x
    for d in range(1, n):
        total = total + lax.ppermute(x, axis, [(j, (j + d) % n) for j in range(n)])
    return total


def per_device(
    hidden, residual, down_projection_weight, adapter_down_maps, adapter_up_maps, row_adapter_index
):
    group_count = 4
    rows, hidden_cols = hidden.shape
    resident_adapters = adapter_down_maps.shape[0]
    adapter_total = resident_adapters * group_count
    per_owner = resident_adapters * MOST
    g = lax.axis_index(GROUP)

    row_adapter = row_adapter_index[:, 0]
    one_hot = (row_adapter[:, None] == jnp.arange(adapter_total, dtype=jnp.int32)[None, :]).astype(
        jnp.int32
    )
    before = jnp.cumsum(one_hot, axis=0) - 1
    slot_rank = jnp.sum(one_hot * before, axis=1)
    slot_index = row_adapter * MOST + slot_rank
    parcels = jnp.zeros((adapter_total * MOST, hidden_cols), jnp.bfloat16).at[slot_index].set(hidden)
    parcels = parcels.reshape(group_count, per_owner, hidden_cols)

    shifted = [_pick(parcels, g, 0)]
    for d in range(1, group_count):
        perm = [(j, (j + d) % group_count) for j in range(group_count)]
        shifted.append(lax.ppermute(_pick(parcels, (g + d) % group_count, 0), GROUP, perm))
    mine = jnp.stack(shifted).reshape(group_count, resident_adapters, MOST, hidden_cols)

    half = rows // 2
    w = down_projection_weight
    feature_blocks = (4, 4, 2, w.shape[1] // 32)

    def partial(h):
        out = lax.dot_general(w, h, (((0,), (1,)), ((), ())), preferred_element_type=jnp.float32)
        return out.astype(jnp.bfloat16).reshape(*feature_blocks, h.shape[0])

    part_a = partial(hidden[:half])
    part_b = partial(hidden[half:])

    partial_mix = jnp.einsum(
        "dlmf,lrf->dlmr", mine, adapter_down_maps, preferred_element_type=jnp.float32
    )

    red_a = reduce_scatter_axis(part_a, "z", 4, 0)
    red_b = reduce_scatter_axis(part_b, "y", 4, 1)
    red_a = reduce_scatter_axis(red_a, "y", 4, 0)
    red_b = reduce_scatter_axis(red_b, "z", 4, 0)
    both = jnp.concatenate([red_a, red_b], axis=-1)
    base_cols = reduce_scatter_axis(both, "xl", 2, 0, out_f32=True)

    mix = partial_mix
    for axis, n in (("z", 4), ("y", 4), ("xl", 2)):
        mix = all_reduce_axis(mix, axis, n)
    rank_mix = mix.astype(jnp.bfloat16)
    delta_mine = jnp.einsum(
        "dlmr,lrc->dlmc", rank_mix, adapter_up_maps, preferred_element_type=jnp.float32
    ).astype(jnp.bfloat16)
    feature_cols = delta_mine.shape[-1]
    delta_mine = delta_mine.reshape(group_count, per_owner, feature_cols)

    back = [delta_mine[0]]
    for d in range(1, group_count):
        perm = [(j, (j - d) % group_count) for j in range(group_count)]
        back.append(lax.ppermute(delta_mine[d], GROUP, perm))
    back = jnp.stack(back).reshape(group_count * per_owner, feature_cols)
    owner = slot_index // per_owner
    place = ((owner - g) % group_count) * per_owner + slot_index % per_owner
    delta_rows = back[place]

    total = residual.astype(jnp.float32) + base_cols.T + delta_rows.astype(jnp.float32)
    return total.astype(jnp.bfloat16)


def solution(mesh):
    fine = Mesh(mesh.devices.reshape(2, 2, 4, 4, 2), GROUP + TP)
    in_specs = (
        P(GROUP, TP),
        P(GROUP, TP),
        P(TP, None),
        P(GROUP, None, TP),
        P(GROUP, None, TP),
        P(GROUP, None),
    )
    out_specs = P(GROUP, TP)
    return jax.shard_map(
        per_device, mesh=fine, in_specs=in_specs, out_specs=out_specs, check_vma=False
    )
```

```python
import jax
import jax.numpy as jnp
from jax import lax
from jax.sharding import Mesh
from jax.sharding import PartitionSpec as P

MOST = 16
GROUP = ("xh", "c")
TP = ("z", "y", "xl")


def _pick(x, k, dim):
    return lax.dynamic_index_in_dim(x, k, dim, keepdims=False)


def _combine(blocks, axis, n, out_f32):
    i = lax.axis_index(axis)
    f32 = jnp.float32
    if n == 2:
        recv = lax.ppermute(blocks(1 - i), axis, [(0, 1), (1, 0)])
        total = recv.astype(f32) + blocks(i).astype(f32)
        return total if out_f32 else total.astype(jnp.bfloat16)
    fw = [(j, (j + 1) % n) for j in range(n)]
    bw = [(j, (j - 1) % n) for j in range(n)]
    far = blocks((i + 2) % n)
    h = far.shape[0] // 2
    got_a = lax.ppermute(far[:h], axis, fw)
    got_b = lax.ppermute(far[h:], axis, bw)
    nxt = blocks((i + 1) % n)
    prv = blocks((i - 1) % n)
    to_next = jnp.concatenate(
        [(nxt[:h].astype(f32) + got_a.astype(f32)).astype(jnp.bfloat16), nxt[h:]], axis=0
    )
    to_prev = jnp.concatenate(
        [prv[:h], (prv[h:].astype(f32) + got_b.astype(f32)).astype(jnp.bfloat16)], axis=0
    )
    from_prev = lax.ppermute(to_next, axis, fw)
    from_next = lax.ppermute(to_prev, axis, bw)
    total = from_prev.astype(f32) + from_next.astype(f32) + blocks(i).astype(f32)
    return total if out_f32 else total.astype(jnp.bfloat16)


def reduce_scatter_axis(x, axis, n, dim=0, out_f32=False):
    return _combine(lambda k: _pick(x, k, dim), axis, n, out_f32)


def all_reduce_axis(x, axis, n):
    total = x
    sent = x.astype(jnp.bfloat16)
    for d in range(1, n):
        total = total + lax.ppermute(sent, axis, [(j, (j + d) % n) for j in range(n)]).astype(jnp.float32)
    return total


def per_device(
    hidden, residual, down_projection_weight, adapter_down_maps, adapter_up_maps, row_adapter_index
):
    group_count = 4
    rows, hidden_cols = hidden.shape
    resident_adapters = adapter_down_maps.shape[0]
    adapter_total = resident_adapters * group_count
    per_owner = resident_adapters * MOST
    g = lax.axis_index(GROUP)

    row_adapter = row_adapter_index[:, 0]
    one_hot = (row_adapter[:, None] == jnp.arange(adapter_total, dtype=jnp.int32)[None, :]).astype(
        jnp.int32
    )
    before = jnp.cumsum(one_hot, axis=0) - 1
    slot_rank = jnp.sum(one_hot * before, axis=1)
    slot_index = row_adapter * MOST + slot_rank
    parcels = jnp.zeros((adapter_total * MOST, hidden_cols), jnp.bfloat16).at[slot_index].set(hidden)
    parcels = parcels.reshape(group_count, per_owner, hidden_cols)

    shifted = [_pick(parcels, g, 0)]
    for d in range(1, group_count):
        perm = [(j, (j + d) % group_count) for j in range(group_count)]
        shifted.append(lax.ppermute(_pick(parcels, (g + d) % group_count, 0), GROUP, perm))
    mine = jnp.stack(shifted).reshape(group_count, resident_adapters, MOST, hidden_cols)

    half = rows // 2
    w = down_projection_weight
    width = w.shape[1]
    tile = width // 32
    w_by_y = w.reshape(hidden_cols, 4, 4, 2 * tile)

    def dot_t(w_cols, h):
        out = lax.dot_general(w_cols, h, (((0,), (1,)), ((), ())), preferred_element_type=jnp.float32)
        return out.astype(jnp.bfloat16)

    h_a, h_b = hidden[:half], hidden[half:]

    def block_z(k):
        cols = lax.dynamic_slice_in_dim(w, k * (width // 4), width // 4, 1)
        return dot_t(cols, h_a).reshape(4, 2, tile, half)

    def block_y(k):
        cols = _pick(w_by_y, k, 2).reshape(hidden_cols, width // 4)
        return dot_t(cols, h_b).reshape(4, 2, tile, half)

    partial_mix = jnp.einsum(
        "dlmf,lrf->dlmr", mine, adapter_down_maps, preferred_element_type=jnp.float32
    )

    red_a = _combine(block_z, "z", 4, False)
    red_b = _combine(block_y, "y", 4, False)
    red_a = reduce_scatter_axis(red_a, "y", 4, 0)
    red_b = reduce_scatter_axis(red_b, "z", 4, 0)
    both = jnp.concatenate([red_a, red_b], axis=-1)
    base_cols = reduce_scatter_axis(both, "xl", 2, 0, out_f32=True)

    mix = partial_mix
    for axis, n in (("xl", 2), ("z", 4), ("y", 4)):
        mix = all_reduce_axis(mix, axis, n)
    rank_mix = mix.astype(jnp.bfloat16)
    delta_mine = jnp.einsum(
        "dlmr,lrc->dlmc", rank_mix, adapter_up_maps, preferred_element_type=jnp.float32
    ).astype(jnp.bfloat16)
    feature_cols = delta_mine.shape[-1]
    delta_mine = delta_mine.reshape(group_count, per_owner, feature_cols)

    back = [delta_mine[0]]
    for d in range(1, group_count):
        perm = [(j, (j - d) % group_count) for j in range(group_count)]
        back.append(lax.ppermute(delta_mine[d], GROUP, perm))
    back = jnp.stack(back).reshape(group_count * per_owner, feature_cols)
    owner = slot_index // per_owner
    place = ((owner - g) % group_count) * per_owner + slot_index % per_owner
    delta_rows = back[place]

    total = residual.astype(jnp.float32) + base_cols.T + delta_rows.astype(jnp.float32)
    return total.astype(jnp.bfloat16)


def solution(mesh):
    fine = Mesh(mesh.devices.reshape(2, 2, 4, 4, 2), GROUP + TP)
    in_specs = (
        P(GROUP, TP),
        P(GROUP, TP),
        P(TP, None),
        P(GROUP, None, TP),
        P(GROUP, None, TP),
        P(GROUP, None),
    )
    out_specs = P(GROUP, TP)
    return jax.shard_map(
        per_device, mesh=fine, in_specs=in_specs, out_specs=out_specs, check_vma=False
    )
```

```python
import jax
import jax.numpy as jnp
from jax import lax
from jax.experimental import pallas as pl
from jax.experimental.pallas import tpu as pltpu
from jax.sharding import Mesh
from jax.sharding import PartitionSpec as P

MOST = 16
GROUP = ("xh", "c")
TP = ("z", "y", "xl")


def _pick(x, k, dim):
    return lax.dynamic_index_in_dim(x, k, dim, keepdims=False)


TILE = 512


def feature_tiles(h, w, base, stride, count):
    rows, depth = h.shape

    def kernel(base_ref, h_ref, w_ref, o_ref):
        o_ref[...] = jnp.dot(h_ref[...], w_ref[...], preferred_element_type=jnp.float32).astype(o_ref.dtype)

    return pl.pallas_call(
        kernel,
        out_shape=jax.ShapeDtypeStruct((rows, count * TILE), jnp.bfloat16),
        grid_spec=pltpu.PrefetchScalarGridSpec(
            num_scalar_prefetch=1,
            grid=(count,),
            in_specs=[
                pl.BlockSpec((rows, depth), lambda t, b: (0, 0)),
                pl.BlockSpec((depth, TILE), lambda t, b: (0, b[0] + t * stride)),
            ],
            out_specs=pl.BlockSpec((rows, TILE), lambda t, b: (0, t)),
        ),
        cost_estimate=pl.CostEstimate(
            flops=2 * rows * depth * TILE * count,
            bytes_accessed=2 * (rows * depth + depth * TILE * count + rows * TILE * count),
            transcendentals=0,
        ),
    )(jnp.reshape(base, (1,)).astype(jnp.int32), h, w)


def _ring_stage(far_a, far_b, nxt, prv, own, axis, out_f32, dim):
    f32 = jnp.float32
    n = 4
    fw = [(j, (j + 1) % n) for j in range(n)]
    bw = [(j, (j - 1) % n) for j in range(n)]
    h = far_a.shape[dim]
    got_a = lax.ppermute(far_a, axis, fw)
    got_b = lax.ppermute(far_b, axis, bw)
    lo = lambda x: lax.slice_in_dim(x, 0, h, axis=dim)
    hi = lambda x: lax.slice_in_dim(x, h, 2 * h, axis=dim)
    to_next = jnp.concatenate(
        [(lo(nxt).astype(f32) + got_a.astype(f32)).astype(jnp.bfloat16), hi(nxt)], axis=dim
    )
    to_prev = jnp.concatenate(
        [lo(prv), (hi(prv).astype(f32) + got_b.astype(f32)).astype(jnp.bfloat16)], axis=dim
    )
    from_prev = lax.ppermute(to_next, axis, fw)
    from_next = lax.ppermute(to_prev, axis, bw)
    total = from_prev.astype(f32) + from_next.astype(f32) + own.astype(f32)
    return total if out_f32 else total.astype(jnp.bfloat16)


def reduce_scatter_axis(x, axis, n, dim, out_f32=False):
    i = lax.axis_index(axis)
    if n == 2:
        recv = lax.ppermute(_pick(x, 1 - i, dim), axis, [(0, 1), (1, 0)])
        total = recv.astype(jnp.float32) + _pick(x, i, dim).astype(jnp.float32)
        return total if out_f32 else total.astype(jnp.bfloat16)
    far = _pick(x, (i + 2) % n, dim)
    h = far.shape[dim] // 2
    return _ring_stage(
        lax.slice_in_dim(far, 0, h, axis=dim),
        lax.slice_in_dim(far, h, 2 * h, axis=dim),
        _pick(x, (i + 1) % n, dim),
        _pick(x, (i - 1) % n, dim),
        _pick(x, i, dim),
        axis,
        out_f32,
        dim,
    )


def all_reduce_axis(x, axis, n):
    total = x
    sent = x.astype(jnp.bfloat16)
    for d in range(1, n):
        total = total + lax.ppermute(sent, axis, [(j, (j + d) % n) for j in range(n)]).astype(jnp.float32)
    return total


def per_device(
    hidden, residual, down_projection_weight, adapter_down_maps, adapter_up_maps, row_adapter_index
):
    group_count = 4
    rows, hidden_cols = hidden.shape
    resident_adapters = adapter_down_maps.shape[0]
    adapter_total = resident_adapters * group_count
    per_owner = resident_adapters * MOST
    g = lax.axis_index(GROUP)

    row_adapter = row_adapter_index[:, 0]
    one_hot = (row_adapter[:, None] == jnp.arange(adapter_total, dtype=jnp.int32)[None, :]).astype(
        jnp.int32
    )
    before = jnp.cumsum(one_hot, axis=0) - 1
    slot_rank = jnp.sum(one_hot * before, axis=1)
    slot_index = row_adapter * MOST + slot_rank
    parcels = jnp.zeros((adapter_total * MOST, hidden_cols), jnp.bfloat16).at[slot_index].set(hidden)
    parcels = parcels.reshape(group_count, per_owner, hidden_cols)

    shifted = [_pick(parcels, g, 0)]
    for d in range(1, group_count):
        perm = [(j, (j + d) % group_count) for j in range(group_count)]
        shifted.append(lax.ppermute(_pick(parcels, (g + d) % group_count, 0), GROUP, perm))
    mine = jnp.stack(shifted).reshape(group_count, resident_adapters, MOST, hidden_cols)

    half = rows // 2
    w = down_projection_weight
    per_z = w.shape[1] // 4 // TILE
    h_a, h_b = hidden[:half], hidden[half:]
    iz, iy = lax.axis_index("z"), lax.axis_index("y")

    def z_block(k, first=0, count=per_z):
        return feature_tiles(h_a, w, k * per_z + first, 1, count)

    def y_block(k, first=0, count=per_z):
        return feature_tiles(h_b, w, k + first * per_z, per_z, count)

    def stage_one(block, i, axis):
        far = (i + 2) % 4
        hc = per_z // 2
        return _ring_stage(
            block(far, 0, hc), block(far, hc, hc), block((i + 1) % 4), block((i - 1) % 4), block(i),
            axis, False, 1,
        )

    partial_mix = jnp.einsum(
        "dlmf,lrf->dlmr", mine, adapter_down_maps, preferred_element_type=jnp.float32
    )

    tile = w.shape[1] // 32
    red_a = stage_one(z_block, iz, "z").reshape(half, 4, 2, tile)
    red_b = stage_one(y_block, iy, "y").reshape(half, 4, 2, tile)
    red_a = reduce_scatter_axis(red_a, "y", 4, 1)
    red_b = reduce_scatter_axis(red_b, "z", 4, 1)
    both = jnp.concatenate([red_a, red_b], axis=0)
    base_rows = reduce_scatter_axis(both, "xl", 2, 1, out_f32=True)

    mix = partial_mix
    for axis, n in (("xl", 2), ("z", 4), ("y", 4)):
        mix = all_reduce_axis(mix, axis, n)
    rank_mix = mix.astype(jnp.bfloat16)
    delta_mine = jnp.einsum(
        "dlmr,lrc->dlmc", rank_mix, adapter_up_maps, preferred_element_type=jnp.float32
    ).astype(jnp.bfloat16)
    feature_cols = delta_mine.shape[-1]
    delta_mine = delta_mine.reshape(group_count, per_owner, feature_cols)

    back = [delta_mine[0]]
    for d in range(1, group_count):
        perm = [(j, (j - d) % group_count) for j in range(group_count)]
        back.append(lax.ppermute(delta_mine[d], GROUP, perm))
    back = jnp.stack(back).reshape(group_count * per_owner, feature_cols)
    owner = slot_index // per_owner
    place = ((owner - g) % group_count) * per_owner + slot_index % per_owner
    delta_rows = back[place]

    total = residual.astype(jnp.float32) + base_rows + delta_rows.astype(jnp.float32)
    return total.astype(jnp.bfloat16)


def solution(mesh):
    fine = Mesh(mesh.devices.reshape(2, 2, 4, 4, 2), GROUP + TP)
    in_specs = (
        P(GROUP, TP),
        P(GROUP, TP),
        P(TP, None),
        P(GROUP, None, TP),
        P(GROUP, None, TP),
        P(GROUP, None),
    )
    out_specs = P(GROUP, TP)
    return jax.shard_map(
        per_device, mesh=fine, in_specs=in_specs, out_specs=out_specs, check_vma=False
    )
```

```python
import jax
import jax.numpy as jnp
from jax import lax
from jax.experimental import pallas as pl
from jax.experimental.pallas import tpu as pltpu
from jax.sharding import Mesh
from jax.sharding import PartitionSpec as P

MOST = 16
GROUP = ("xh", "c")
TP = ("z", "y", "xl")


def _pick(x, k, dim):
    return lax.dynamic_index_in_dim(x, k, dim, keepdims=False)


TILE = 512


def feature_tiles(h, w, base, stride, count):
    rows, depth = h.shape

    def kernel(base_ref, h_ref, w_ref, o_ref):
        o_ref[...] = jnp.dot(h_ref[...], w_ref[...], preferred_element_type=jnp.float32).astype(o_ref.dtype)

    return pl.pallas_call(
        kernel,
        out_shape=jax.ShapeDtypeStruct((rows, count * TILE), jnp.bfloat16),
        grid_spec=pltpu.PrefetchScalarGridSpec(
            num_scalar_prefetch=1,
            grid=(count,),
            in_specs=[
                pl.BlockSpec((rows, depth), lambda t, b: (0, 0)),
                pl.BlockSpec((depth, TILE), lambda t, b: (0, b[0] + t * stride)),
            ],
            out_specs=pl.BlockSpec((rows, TILE), lambda t, b: (0, t)),
        ),
        cost_estimate=pl.CostEstimate(
            flops=2 * rows * depth * TILE * count,
            bytes_accessed=2 * (rows * depth + depth * TILE * count + rows * TILE * count),
            transcendentals=0,
        ),
    )(jnp.reshape(base, (1,)).astype(jnp.int32), h, w)


def _ring_stage(far_a, far_b, nxt, prv, own, axis, out_f32, dim):
    f32 = jnp.float32
    n = 4
    fw = [(j, (j + 1) % n) for j in range(n)]
    bw = [(j, (j - 1) % n) for j in range(n)]
    h = far_a.shape[dim]
    got_a = lax.ppermute(far_a, axis, fw)
    got_b = lax.ppermute(far_b, axis, bw)
    lo = lambda x: lax.slice_in_dim(x, 0, h, axis=dim)
    hi = lambda x: lax.slice_in_dim(x, h, 2 * h, axis=dim)
    to_next = jnp.concatenate(
        [(lo(nxt).astype(f32) + got_a.astype(f32)).astype(jnp.bfloat16), hi(nxt)], axis=dim
    )
    to_prev = jnp.concatenate(
        [lo(prv), (hi(prv).astype(f32) + got_b.astype(f32)).astype(jnp.bfloat16)], axis=dim
    )
    from_prev = lax.ppermute(to_next, axis, fw)
    from_next = lax.ppermute(to_prev, axis, bw)
    total = from_prev.astype(f32) + from_next.astype(f32) + own.astype(f32)
    return total if out_f32 else total.astype(jnp.bfloat16)


def reduce_scatter_axis(x, axis, n, out_f32=False):
    i = lax.axis_index(axis)
    width = x.shape[1] // n
    pick = lambda k: lax.dynamic_slice_in_dim(x, k * width, width, axis=1)
    if n == 2:
        recv = lax.ppermute(pick(1 - i), axis, [(0, 1), (1, 0)])
        total = recv.astype(jnp.float32) + pick(i).astype(jnp.float32)
        return total if out_f32 else total.astype(jnp.bfloat16)
    far = pick((i + 2) % n)
    h = width // 2
    return _ring_stage(
        far[:, :h], far[:, h:], pick((i + 1) % n), pick((i - 1) % n), pick(i), axis, out_f32, 1
    )


def all_reduce_axis(x, axis, n):
    total = x
    sent = x.astype(jnp.bfloat16)
    for d in range(1, n):
        total = total + lax.ppermute(sent, axis, [(j, (j + d) % n) for j in range(n)]).astype(jnp.float32)
    return total


def per_device(
    hidden, residual, down_projection_weight, adapter_down_maps, adapter_up_maps, row_adapter_index
):
    group_count = 4
    rows, hidden_cols = hidden.shape
    resident_adapters = adapter_down_maps.shape[0]
    adapter_total = resident_adapters * group_count
    per_owner = resident_adapters * MOST
    g = lax.axis_index(GROUP)

    row_adapter = row_adapter_index[:, 0]
    one_hot = (row_adapter[:, None] == jnp.arange(adapter_total, dtype=jnp.int32)[None, :]).astype(
        jnp.int32
    )
    before = jnp.cumsum(one_hot, axis=0) - 1
    slot_rank = jnp.sum(one_hot * before, axis=1)
    slot_index = row_adapter * MOST + slot_rank
    parcels = jnp.zeros((adapter_total * MOST, hidden_cols), jnp.bfloat16).at[slot_index].set(hidden)
    parcels = parcels.reshape(group_count, per_owner, hidden_cols)

    shifted = [_pick(parcels, g, 0)]
    for d in range(1, group_count):
        perm = [(j, (j + d) % group_count) for j in range(group_count)]
        shifted.append(lax.ppermute(_pick(parcels, (g + d) % group_count, 0), GROUP, perm))
    mine = jnp.stack(shifted).reshape(group_count, resident_adapters, MOST, hidden_cols)

    half = rows // 2
    w = down_projection_weight
    per_z = w.shape[1] // 4 // TILE
    h_a, h_b = hidden[:half], hidden[half:]
    iz, iy = lax.axis_index("z"), lax.axis_index("y")

    def z_block(k, first=0, count=per_z):
        return feature_tiles(h_a, w, k * per_z + first, 1, count)

    def y_block(k, first=0, count=per_z):
        return feature_tiles(h_b, w, k + first * per_z, per_z, count)

    def stage_one(block, i, axis):
        far = (i + 2) % 4
        hc = per_z // 2
        return _ring_stage(
            block(far, 0, hc), block(far, hc, hc), block((i + 1) % 4), block((i - 1) % 4), block(i),
            axis, False, 1,
        )

    partial_mix = jnp.einsum(
        "dlmf,lrf->dlmr", mine, adapter_down_maps, preferred_element_type=jnp.float32
    )

    red_a = reduce_scatter_axis(stage_one(z_block, iz, "z"), "y", 4)
    red_b = reduce_scatter_axis(stage_one(y_block, iy, "y"), "z", 4)
    both = jnp.concatenate([red_a, red_b], axis=0)
    base_rows = reduce_scatter_axis(both, "xl", 2, out_f32=True)

    mix = partial_mix
    for axis, n in (("xl", 2), ("z", 4), ("y", 4)):
        mix = all_reduce_axis(mix, axis, n)
    rank_mix = mix.astype(jnp.bfloat16)
    delta_mine = jnp.einsum(
        "dlmr,lrc->dlmc", rank_mix, adapter_up_maps, preferred_element_type=jnp.float32
    ).astype(jnp.bfloat16)
    feature_cols = delta_mine.shape[-1]
    delta_mine = delta_mine.reshape(group_count, per_owner, feature_cols)

    back = [delta_mine[0]]
    for d in range(1, group_count):
        perm = [(j, (j - d) % group_count) for j in range(group_count)]
        back.append(lax.ppermute(delta_mine[d], GROUP, perm))
    back = jnp.stack(back).reshape(group_count * per_owner, feature_cols)
    owner = slot_index // per_owner
    place = ((owner - g) % group_count) * per_owner + slot_index % per_owner
    delta_rows = back[place]

    total = residual.astype(jnp.float32) + base_rows + delta_rows.astype(jnp.float32)
    return total.astype(jnp.bfloat16)


def solution(mesh):
    fine = Mesh(mesh.devices.reshape(2, 2, 4, 4, 2), GROUP + TP)
    in_specs = (
        P(GROUP, TP),
        P(GROUP, TP),
        P(TP, None),
        P(GROUP, None, TP),
        P(GROUP, None, TP),
        P(GROUP, None),
    )
    out_specs = P(GROUP, TP)
    return jax.shard_map(
        per_device, mesh=fine, in_specs=in_specs, out_specs=out_specs, check_vma=False
    )
```

```python
import jax
import jax.numpy as jnp
from jax import lax
from jax.experimental import pallas as pl
from jax.experimental.pallas import tpu as pltpu
from jax.sharding import Mesh
from jax.sharding import PartitionSpec as P

MOST = 16
GROUP = ("xh", "c")
TP = ("z", "y", "xl")


def _pick(x, k, dim):
    return lax.dynamic_index_in_dim(x, k, dim, keepdims=False)


TILE = 512


def feature_tiles(h, w, base, stride, count, tile=TILE):
    rows, depth = h.shape

    def kernel(base_ref, h_ref, w_ref, o_ref):
        o_ref[...] = jnp.dot(h_ref[...], w_ref[...], preferred_element_type=jnp.float32).astype(o_ref.dtype)

    return pl.pallas_call(
        kernel,
        out_shape=jax.ShapeDtypeStruct((rows, count * tile), jnp.bfloat16),
        grid_spec=pltpu.PrefetchScalarGridSpec(
            num_scalar_prefetch=1,
            grid=(count,),
            in_specs=[
                pl.BlockSpec((rows, depth), lambda t, b: (0, 0)),
                pl.BlockSpec((depth, tile), lambda t, b: (0, b[0] + t * stride)),
            ],
            out_specs=pl.BlockSpec((rows, tile), lambda t, b: (0, t)),
        ),
        cost_estimate=pl.CostEstimate(
            flops=2 * rows * depth * tile * count,
            bytes_accessed=2 * (rows * depth + depth * tile * count + rows * tile * count),
            transcendentals=0,
        ),
    )(jnp.reshape(base, (1,)).astype(jnp.int32), h, w)


def _ring_stage(far_a, far_b, nxt, prv, own, axis, out_f32, dim):
    f32 = jnp.float32
    n = 4
    fw = [(j, (j + 1) % n) for j in range(n)]
    bw = [(j, (j - 1) % n) for j in range(n)]
    h = far_a.shape[dim]
    got_a = lax.ppermute(far_a, axis, fw)
    got_b = lax.ppermute(far_b, axis, bw)
    lo = lambda x: lax.slice_in_dim(x, 0, h, axis=dim)
    hi = lambda x: lax.slice_in_dim(x, h, 2 * h, axis=dim)
    to_next = jnp.concatenate(
        [(lo(nxt).astype(f32) + got_a.astype(f32)).astype(jnp.bfloat16), hi(nxt)], axis=dim
    )
    to_prev = jnp.concatenate(
        [lo(prv), (hi(prv).astype(f32) + got_b.astype(f32)).astype(jnp.bfloat16)], axis=dim
    )
    from_prev = lax.ppermute(to_next, axis, fw)
    from_next = lax.ppermute(to_prev, axis, bw)
    total = from_prev.astype(f32) + from_next.astype(f32) + own.astype(f32)
    return total if out_f32 else total.astype(jnp.bfloat16)


def reduce_scatter_axis(x, axis, n, out_f32=False):
    i = lax.axis_index(axis)
    width = x.shape[1] // n
    pick = lambda k: lax.dynamic_slice_in_dim(x, k * width, width, axis=1)
    if n == 2:
        recv = lax.ppermute(pick(1 - i), axis, [(0, 1), (1, 0)])
        total = recv.astype(jnp.float32) + pick(i).astype(jnp.float32)
        return total if out_f32 else total.astype(jnp.bfloat16)
    far = pick((i + 2) % n)
    h = width // 2
    return _ring_stage(
        far[:, :h], far[:, h:], pick((i + 1) % n), pick((i - 1) % n), pick(i), axis, out_f32, 1
    )


def all_reduce_axis(x, axis, n):
    total = x
    sent = x.astype(jnp.bfloat16)
    for d in range(1, n):
        total = total + lax.ppermute(sent, axis, [(j, (j + d) % n) for j in range(n)]).astype(jnp.float32)
    return total


def per_device(
    hidden, residual, down_projection_weight, adapter_down_maps, adapter_up_maps, row_adapter_index
):
    group_count = 4
    rows, hidden_cols = hidden.shape
    resident_adapters = adapter_down_maps.shape[0]
    adapter_total = resident_adapters * group_count
    per_owner = resident_adapters * MOST
    g = lax.axis_index(GROUP)

    row_adapter = row_adapter_index[:, 0]
    one_hot = (row_adapter[:, None] == jnp.arange(adapter_total, dtype=jnp.int32)[None, :]).astype(
        jnp.int32
    )
    before = jnp.cumsum(one_hot, axis=0) - 1
    slot_rank = jnp.sum(one_hot * before, axis=1)
    slot_index = row_adapter * MOST + slot_rank
    filler = jnp.zeros((adapter_total * MOST,), jnp.int32).at[slot_index].set(
        jnp.arange(rows, dtype=jnp.int32)
    )
    filler = filler.reshape(group_count, per_owner)

    def parcel(owner_group):
        return hidden[_pick(filler, owner_group, 0)]

    shifted = [parcel(g)]
    for d in range(1, group_count):
        perm = [(j, (j + d) % group_count) for j in range(group_count)]
        shifted.append(lax.ppermute(parcel((g + d) % group_count), GROUP, perm))
    mine = jnp.stack(shifted).reshape(group_count, resident_adapters, MOST, hidden_cols)

    half = rows // 2
    w = down_projection_weight
    per_z = w.shape[1] // 4 // TILE
    h_a, h_b = hidden[:half], hidden[half:]
    iz, iy = lax.axis_index("z"), lax.axis_index("y")

    def z_block(k, first=0, count=per_z):
        return feature_tiles(h_a, w, (k * per_z + first) // 2, 1, count // 2, 2 * TILE)

    def y_block(k, first=0, count=per_z):
        return feature_tiles(h_b, w, k + first * per_z, per_z, count)

    def stage_one(block, i, axis):
        far = (i + 2) % 4
        hc = per_z // 2
        return _ring_stage(
            block(far, 0, hc), block(far, hc, hc), block((i + 1) % 4), block((i - 1) % 4), block(i),
            axis, False, 1,
        )

    partial_mix = jnp.einsum(
        "dlmf,lrf->dlmr", mine, adapter_down_maps, preferred_element_type=jnp.float32
    )

    red_a = reduce_scatter_axis(stage_one(z_block, iz, "z"), "y", 4)
    red_b = reduce_scatter_axis(stage_one(y_block, iy, "y"), "z", 4)
    both = jnp.concatenate([red_a, red_b], axis=0)
    base_rows = reduce_scatter_axis(both, "xl", 2, out_f32=True)

    mix = partial_mix
    for axis, n in (("xl", 2), ("z", 4), ("y", 4)):
        mix = all_reduce_axis(mix, axis, n)
    rank_mix = mix.astype(jnp.bfloat16)
    delta_mine = jnp.einsum(
        "dlmr,lrc->dlmc", rank_mix, adapter_up_maps, preferred_element_type=jnp.float32
    ).astype(jnp.bfloat16)
    feature_cols = delta_mine.shape[-1]
    delta_mine = delta_mine.reshape(group_count, per_owner, feature_cols)

    back = [delta_mine[0]]
    for d in range(1, group_count):
        perm = [(j, (j - d) % group_count) for j in range(group_count)]
        back.append(lax.ppermute(delta_mine[d], GROUP, perm))
    back = jnp.stack(back).reshape(group_count * per_owner, feature_cols)
    owner = slot_index // per_owner
    place = ((owner - g) % group_count) * per_owner + slot_index % per_owner
    delta_rows = back[place]

    total = residual.astype(jnp.float32) + base_rows + delta_rows.astype(jnp.float32)
    return total.astype(jnp.bfloat16)


def solution(mesh):
    fine = Mesh(mesh.devices.reshape(2, 2, 4, 4, 2), GROUP + TP)
    in_specs = (
        P(GROUP, TP),
        P(GROUP, TP),
        P(TP, None),
        P(GROUP, None, TP),
        P(GROUP, None, TP),
        P(GROUP, None),
    )
    out_specs = P(GROUP, TP)
    return jax.shard_map(
        per_device, mesh=fine, in_specs=in_specs, out_specs=out_specs, check_vma=False
    )
```

```python
import jax
import jax.numpy as jnp
from jax import lax
from jax.experimental import pallas as pl
from jax.experimental.pallas import tpu as pltpu
from jax.sharding import Mesh
from jax.sharding import PartitionSpec as P

MOST = 16
GROUP = ("xh", "c")
TP = ("z", "y", "xl")


def _pick(x, k, dim):
    return lax.dynamic_index_in_dim(x, k, dim, keepdims=False)


TILE = 512


def feature_tiles(h, w, base, stride, count, tile=TILE):
    rows, depth = h.shape

    def kernel(base_ref, h_ref, w_ref, o_ref):
        o_ref[...] = jnp.dot(h_ref[...], w_ref[...], preferred_element_type=jnp.float32).astype(o_ref.dtype)

    return pl.pallas_call(
        kernel,
        out_shape=jax.ShapeDtypeStruct((rows, count * tile), jnp.bfloat16),
        grid_spec=pltpu.PrefetchScalarGridSpec(
            num_scalar_prefetch=1,
            grid=(count,),
            in_specs=[
                pl.BlockSpec((rows, depth), lambda t, b: (0, 0)),
                pl.BlockSpec((depth, tile), lambda t, b: (0, b[0] + t * stride)),
            ],
            out_specs=pl.BlockSpec((rows, tile), lambda t, b: (0, t)),
        ),
        cost_estimate=pl.CostEstimate(
            flops=2 * rows * depth * tile * count,
            bytes_accessed=2 * (rows * depth + depth * tile * count + rows * tile * count),
            transcendentals=0,
        ),
    )(jnp.reshape(base, (1,)).astype(jnp.int32), h, w)


def _ring_stage(far_a, far_b, nxt, prv, own, axis, out_f32, dim):
    f32 = jnp.float32
    n = 4
    fw = [(j, (j + 1) % n) for j in range(n)]
    bw = [(j, (j - 1) % n) for j in range(n)]
    h = far_a.shape[dim]
    got_a = lax.ppermute(far_a, axis, fw)
    got_b = lax.ppermute(far_b, axis, bw)
    lo = lambda x: lax.slice_in_dim(x, 0, h, axis=dim)
    hi = lambda x: lax.slice_in_dim(x, h, 2 * h, axis=dim)
    to_next = jnp.concatenate(
        [(lo(nxt).astype(f32) + got_a.astype(f32)).astype(jnp.bfloat16), hi(nxt)], axis=dim
    )
    to_prev = jnp.concatenate(
        [lo(prv), (hi(prv).astype(f32) + got_b.astype(f32)).astype(jnp.bfloat16)], axis=dim
    )
    from_prev = lax.ppermute(to_next, axis, fw)
    from_next = lax.ppermute(to_prev, axis, bw)
    total = from_prev.astype(f32) + from_next.astype(f32) + own.astype(f32)
    return total if out_f32 else total.astype(jnp.bfloat16)


def reduce_scatter_axis(x, axis, n, out_f32=False):
    i = lax.axis_index(axis)
    width = x.shape[1] // n
    pick = lambda k: lax.dynamic_slice_in_dim(x, k * width, width, axis=1)
    if n == 2:
        recv = lax.ppermute(pick(1 - i), axis, [(0, 1), (1, 0)])
        total = recv.astype(jnp.float32) + pick(i).astype(jnp.float32)
        return total if out_f32 else total.astype(jnp.bfloat16)
    far = pick((i + 2) % n)
    h = width // 2
    return _ring_stage(
        far[:, :h], far[:, h:], pick((i + 1) % n), pick((i - 1) % n), pick(i), axis, out_f32, 1
    )


def all_reduce_axis(x, axis, n):
    total = x
    sent = x.astype(jnp.bfloat16)
    for d in range(1, n):
        total = total + lax.ppermute(sent, axis, [(j, (j + d) % n) for j in range(n)]).astype(jnp.float32)
    return total


def per_device(
    hidden, residual, down_projection_weight, adapter_down_maps, adapter_up_maps, row_adapter_index
):
    group_count = 4
    rows, hidden_cols = hidden.shape
    resident_adapters = adapter_down_maps.shape[0]
    adapter_total = resident_adapters * group_count
    per_owner = resident_adapters * MOST
    g = lax.axis_index(GROUP)

    row_adapter = row_adapter_index[:, 0]
    one_hot = (row_adapter[:, None] == jnp.arange(adapter_total, dtype=jnp.int32)[None, :]).astype(
        jnp.int32
    )
    before = jnp.cumsum(one_hot, axis=0) - 1
    slot_rank = jnp.sum(one_hot * before, axis=1)
    slot_index = row_adapter * MOST + slot_rank
    parcels = jnp.zeros((adapter_total * MOST, hidden_cols), jnp.bfloat16).at[slot_index].set(hidden)
    parcels = parcels.reshape(group_count, per_owner, hidden_cols)

    shifted = [_pick(parcels, g, 0)]
    for d in range(1, group_count):
        perm = [(j, (j + d) % group_count) for j in range(group_count)]
        shifted.append(lax.ppermute(_pick(parcels, (g + d) % group_count, 0), GROUP, perm))
    mine = jnp.stack(shifted).reshape(group_count, resident_adapters, MOST, hidden_cols)

    every_up = lax.all_gather(adapter_up_maps, GROUP, axis=0, tiled=True)

    half = rows // 2
    w = down_projection_weight
    per_z = w.shape[1] // 4 // TILE
    h_a, h_b = hidden[:half], hidden[half:]
    iz, iy = lax.axis_index("z"), lax.axis_index("y")

    def z_block(k, first=0, count=per_z):
        return feature_tiles(h_a, w, (k * per_z + first) // 2, 1, count // 2, 2 * TILE)

    def y_block(k, first=0, count=per_z):
        return feature_tiles(h_b, w, k + first * per_z, per_z, count)

    def stage_one(block, i, axis):
        far = (i + 2) % 4
        hc = per_z // 2
        return _ring_stage(
            block(far, 0, hc), block(far, hc, hc), block((i + 1) % 4), block((i - 1) % 4), block(i),
            axis, False, 1,
        )

    partial_mix = jnp.einsum(
        "dlmf,lrf->dlmr", mine, adapter_down_maps, preferred_element_type=jnp.float32
    )

    red_a = reduce_scatter_axis(stage_one(z_block, iz, "z"), "y", 4)
    red_b = reduce_scatter_axis(stage_one(y_block, iy, "y"), "z", 4)
    both = jnp.concatenate([red_a, red_b], axis=0)
    base_rows = reduce_scatter_axis(both, "xl", 2, out_f32=True)

    mix = partial_mix
    for axis, n in (("xl", 2), ("z", 4), ("y", 4)):
        mix = all_reduce_axis(mix, axis, n)
    rank_mix = mix.astype(jnp.bfloat16).reshape(group_count, per_owner, -1)

    back = [rank_mix[0]]
    for d in range(1, group_count):
        perm = [(j, (j - d) % group_count) for j in range(group_count)]
        back.append(lax.ppermute(rank_mix[d], GROUP, perm))
    back = jnp.stack(back)
    by_owner = jnp.stack([_pick(back, (o - g) % group_count, 0) for o in range(group_count)])
    by_owner = by_owner.reshape(adapter_total, MOST, -1)
    delta_slots = jnp.einsum(
        "amr,ard->amd", by_owner, every_up, preferred_element_type=jnp.float32
    ).astype(jnp.bfloat16)
    delta_rows = delta_slots.reshape(adapter_total * MOST, -1)[slot_index]

    total = residual.astype(jnp.float32) + base_rows + delta_rows.astype(jnp.float32)
    return total.astype(jnp.bfloat16)


def solution(mesh):
    fine = Mesh(mesh.devices.reshape(2, 2, 4, 4, 2), GROUP + TP)
    in_specs = (
        P(GROUP, TP),
        P(GROUP, TP),
        P(TP, None),
        P(GROUP, None, TP),
        P(GROUP, None, TP),
        P(GROUP, None),
    )
    out_specs = P(GROUP, TP)
    return jax.shard_map(
        per_device, mesh=fine, in_specs=in_specs, out_specs=out_specs, check_vma=False
    )
```

```python
import jax
import jax.numpy as jnp
from jax import lax
from jax.experimental import pallas as pl
from jax.experimental.pallas import tpu as pltpu
from jax.sharding import Mesh
from jax.sharding import PartitionSpec as P

MOST = 16
GROUP = ("xh", "c")
TP = ("z", "y", "xl")


def _pick(x, k, dim):
    return lax.dynamic_index_in_dim(x, k, dim, keepdims=False)


TILE = 512


def feature_tiles(h, w, base, stride, count):
    rows, depth = h.shape

    def kernel(base_ref, h_ref, w_ref, o_ref):
        o_ref[...] = jnp.dot(h_ref[...], w_ref[...], preferred_element_type=jnp.float32).astype(o_ref.dtype)

    return pl.pallas_call(
        kernel,
        out_shape=jax.ShapeDtypeStruct((rows, count * TILE), jnp.bfloat16),
        grid_spec=pltpu.PrefetchScalarGridSpec(
            num_scalar_prefetch=1,
            grid=(count,),
            in_specs=[
                pl.BlockSpec((rows, depth), lambda t, b: (0, 0)),
                pl.BlockSpec((depth, TILE), lambda t, b: (0, b[0] + t * stride)),
            ],
            out_specs=pl.BlockSpec((rows, TILE), lambda t, b: (0, t)),
        ),
        cost_estimate=pl.CostEstimate(
            flops=2 * rows * depth * TILE * count,
            bytes_accessed=2 * (rows * depth + depth * TILE * count + rows * TILE * count),
            transcendentals=0,
        ),
    )(jnp.reshape(base, (1,)).astype(jnp.int32), h, w)


def _ring_stage(far_a, far_b, nxt, prv, own, axis, out_f32, dim):
    f32 = jnp.float32
    n = 4
    fw = [(j, (j + 1) % n) for j in range(n)]
    bw = [(j, (j - 1) % n) for j in range(n)]
    h = far_a.shape[dim]
    got_a = lax.ppermute(far_a, axis, fw)
    got_b = lax.ppermute(far_b, axis, bw)
    lo = lambda x: lax.slice_in_dim(x, 0, h, axis=dim)
    hi = lambda x: lax.slice_in_dim(x, h, 2 * h, axis=dim)
    to_next = jnp.concatenate(
        [(lo(nxt).astype(f32) + got_a.astype(f32)).astype(jnp.bfloat16), hi(nxt)], axis=dim
    )
    to_prev = jnp.concatenate(
        [lo(prv), (hi(prv).astype(f32) + got_b.astype(f32)).astype(jnp.bfloat16)], axis=dim
    )
    from_prev = lax.ppermute(to_next, axis, fw)
    from_next = lax.ppermute(to_prev, axis, bw)
    total = from_prev.astype(f32) + from_next.astype(f32) + own.astype(f32)
    return total if out_f32 else total.astype(jnp.bfloat16)


def reduce_scatter_axis(x, axis, n, out_f32=False):
    i = lax.axis_index(axis)
    width = x.shape[1] // n
    pick = lambda k: lax.dynamic_slice_in_dim(x, k * width, width, axis=1)
    if n == 2:
        recv = lax.ppermute(pick(1 - i), axis, [(0, 1), (1, 0)])
        total = recv.astype(jnp.float32) + pick(i).astype(jnp.float32)
        return total if out_f32 else total.astype(jnp.bfloat16)
    far = pick((i + 2) % n)
    h = width // 2
    return _ring_stage(
        far[:, :h], far[:, h:], pick((i + 1) % n), pick((i - 1) % n), pick(i), axis, out_f32, 1
    )


def all_reduce_axis(x, axis, n):
    total = x
    sent = x.astype(jnp.bfloat16)
    for d in range(1, n):
        total = total + lax.ppermute(sent, axis, [(j, (j + d) % n) for j in range(n)]).astype(jnp.float32)
    return total


def per_device(
    hidden, residual, down_projection_weight, adapter_down_maps, adapter_up_maps, row_adapter_index
):
    group_count = 4
    rows, hidden_cols = hidden.shape
    resident_adapters = adapter_down_maps.shape[0]
    adapter_total = resident_adapters * group_count
    per_owner = resident_adapters * MOST
    g = lax.axis_index(GROUP)

    row_adapter = row_adapter_index[:, 0]
    one_hot = (row_adapter[:, None] == jnp.arange(adapter_total, dtype=jnp.int32)[None, :]).astype(
        jnp.int32
    )
    before = jnp.cumsum(one_hot, axis=0) - 1
    slot_rank = jnp.sum(one_hot * before, axis=1)
    slot_index = row_adapter * MOST + slot_rank
    parcels = jnp.zeros((adapter_total * MOST, hidden_cols), jnp.bfloat16).at[slot_index].set(hidden)
    parcels = parcels.reshape(group_count, per_owner, hidden_cols)

    shifted = [_pick(parcels, g, 0)]
    for d in range(1, group_count):
        perm = [(j, (j + d) % group_count) for j in range(group_count)]
        shifted.append(lax.ppermute(_pick(parcels, (g + d) % group_count, 0), GROUP, perm))
    mine = jnp.stack(shifted).reshape(group_count, resident_adapters, MOST, hidden_cols)

    half = rows // 2
    w = down_projection_weight
    per_z = w.shape[1] // 4 // TILE
    h_a, h_b = hidden[:half], hidden[half:]
    iz, iy = lax.axis_index("z"), lax.axis_index("y")

    def z_block(k, first=0, count=per_z):
        return feature_tiles(h_a, w, k * per_z + first, 1, count)

    def y_block(k, first=0, count=per_z):
        return feature_tiles(h_b, w, k + first * per_z, per_z, count)

    def stage_one(block, i, axis):
        far = (i + 2) % 4
        hc = per_z // 2
        return _ring_stage(
            block(far, 0, hc), block(far, hc, hc), block((i + 1) % 4), block((i - 1) % 4), block(i),
            axis, False, 1,
        )

    partial_mix = jnp.einsum(
        "dlmf,lrf->dlmr", mine, adapter_down_maps, preferred_element_type=jnp.float32
    )

    red_a = reduce_scatter_axis(stage_one(z_block, iz, "z"), "y", 4)
    red_b = reduce_scatter_axis(stage_one(y_block, iy, "y"), "z", 4)
    base_rows = jnp.concatenate(
        [reduce_scatter_axis(red_a, "xl", 2, out_f32=True), reduce_scatter_axis(red_b, "xl", 2, out_f32=True)],
        axis=0,
    )

    mix = partial_mix
    for axis, n in (("xl", 2), ("z", 4), ("y", 4)):
        mix = all_reduce_axis(mix, axis, n)
    rank_mix = mix.astype(jnp.bfloat16)
    delta_mine = jnp.einsum(
        "dlmr,lrc->dlmc", rank_mix, adapter_up_maps, preferred_element_type=jnp.float32
    ).astype(jnp.bfloat16)
    feature_cols = delta_mine.shape[-1]
    delta_mine = delta_mine.reshape(group_count, per_owner, feature_cols)

    back = [delta_mine[0]]
    for d in range(1, group_count):
        perm = [(j, (j - d) % group_count) for j in range(group_count)]
        back.append(lax.ppermute(delta_mine[d], GROUP, perm))
    back = jnp.stack(back).reshape(group_count * per_owner, feature_cols)
    owner = slot_index // per_owner
    place = ((owner - g) % group_count) * per_owner + slot_index % per_owner
    delta_rows = back[place]

    total = residual.astype(jnp.float32) + base_rows + delta_rows.astype(jnp.float32)
    return total.astype(jnp.bfloat16)


def solution(mesh):
    fine = Mesh(mesh.devices.reshape(2, 2, 4, 4, 2), GROUP + TP)
    in_specs = (
        P(GROUP, TP),
        P(GROUP, TP),
        P(TP, None),
        P(GROUP, None, TP),
        P(GROUP, None, TP),
        P(GROUP, None),
    )
    out_specs = P(GROUP, TP)
    return jax.shard_map(
        per_device, mesh=fine, in_specs=in_specs, out_specs=out_specs, check_vma=False
    )
```

```python
import jax
import jax.numpy as jnp
from jax import lax
from jax.experimental import pallas as pl
from jax.experimental.pallas import tpu as pltpu
from jax.sharding import Mesh
from jax.sharding import PartitionSpec as P

MOST = 16
GROUP = ("xh", "c")
TP = ("z", "y", "xl")


def _pick(x, k, dim):
    return lax.dynamic_index_in_dim(x, k, dim, keepdims=False)


TILE = 512


def feature_tiles(h, w, base, stride, count, tile=TILE):
    rows, depth = h.shape

    def kernel(base_ref, h_ref, w_ref, o_ref):
        o_ref[...] = jnp.dot(h_ref[...], w_ref[...], preferred_element_type=jnp.float32).astype(o_ref.dtype)

    return pl.pallas_call(
        kernel,
        out_shape=jax.ShapeDtypeStruct((rows, count * tile), jnp.bfloat16),
        grid_spec=pltpu.PrefetchScalarGridSpec(
            num_scalar_prefetch=1,
            grid=(count,),
            in_specs=[
                pl.BlockSpec((rows, depth), lambda t, b: (0, 0)),
                pl.BlockSpec((depth, tile), lambda t, b: (0, b[0] + t * stride)),
            ],
            out_specs=pl.BlockSpec((rows, tile), lambda t, b: (0, t)),
        ),
        cost_estimate=pl.CostEstimate(
            flops=2 * rows * depth * tile * count,
            bytes_accessed=2 * (rows * depth + depth * tile * count + rows * tile * count),
            transcendentals=0,
        ),
    )(jnp.reshape(base, (1,)).astype(jnp.int32), h, w)


def _ring_stage(far_a, far_b, nxt, prv, own, axis, out_f32, dim):
    f32 = jnp.float32
    n = 4
    fw = [(j, (j + 1) % n) for j in range(n)]
    bw = [(j, (j - 1) % n) for j in range(n)]
    h = far_a.shape[dim]
    got_a = lax.ppermute(far_a, axis, fw)
    got_b = lax.ppermute(far_b, axis, bw)
    lo = lambda x: lax.slice_in_dim(x, 0, h, axis=dim)
    hi = lambda x: lax.slice_in_dim(x, h, 2 * h, axis=dim)
    to_next = jnp.concatenate(
        [(lo(nxt).astype(f32) + got_a.astype(f32)).astype(jnp.bfloat16), hi(nxt)], axis=dim
    )
    to_prev = jnp.concatenate(
        [lo(prv), (hi(prv).astype(f32) + got_b.astype(f32)).astype(jnp.bfloat16)], axis=dim
    )
    from_prev = lax.ppermute(to_next, axis, fw)
    from_next = lax.ppermute(to_prev, axis, bw)
    total = from_prev.astype(f32) + from_next.astype(f32) + own.astype(f32)
    return total if out_f32 else total.astype(jnp.bfloat16)


def reduce_scatter_axis(x, axis, n, out_f32=False):
    i = lax.axis_index(axis)
    width = x.shape[1] // n
    pick = lambda k: lax.dynamic_slice_in_dim(x, k * width, width, axis=1)
    if n == 2:
        recv = lax.ppermute(pick(1 - i), axis, [(0, 1), (1, 0)])
        total = recv.astype(jnp.float32) + pick(i).astype(jnp.float32)
        return total if out_f32 else total.astype(jnp.bfloat16)
    far = pick((i + 2) % n)
    h = width // 2
    return _ring_stage(
        far[:, :h], far[:, h:], pick((i + 1) % n), pick((i - 1) % n), pick(i), axis, out_f32, 1
    )


def all_reduce_axis(x, axis, n):
    total = x
    sent = x.astype(jnp.bfloat16)
    for d in range(1, n):
        total = total + lax.ppermute(sent, axis, [(j, (j + d) % n) for j in range(n)]).astype(jnp.float32)
    return total


def per_device(
    hidden, residual, down_projection_weight, adapter_down_maps, adapter_up_maps, row_adapter_index
):
    group_count = 4
    rows, hidden_cols = hidden.shape
    resident_adapters = adapter_down_maps.shape[0]
    adapter_total = resident_adapters * group_count
    per_owner = resident_adapters * MOST
    g = lax.axis_index(GROUP)

    row_adapter = row_adapter_index[:, 0]
    one_hot = (row_adapter[:, None] == jnp.arange(adapter_total, dtype=jnp.int32)[None, :]).astype(
        jnp.int32
    )
    before = jnp.cumsum(one_hot, axis=0) - 1
    slot_rank = jnp.sum(one_hot * before, axis=1)
    slot_index = row_adapter * MOST + slot_rank
    parcels = jnp.zeros((adapter_total * MOST, hidden_cols), jnp.bfloat16).at[slot_index].set(hidden)
    parcels = parcels.reshape(group_count, per_owner, hidden_cols)

    shifted = [_pick(parcels, g, 0)]
    for d in range(1, group_count):
        perm = [(j, (j + d) % group_count) for j in range(group_count)]
        shifted.append(lax.ppermute(_pick(parcels, (g + d) % group_count, 0), GROUP, perm))
    mine = jnp.stack(shifted).reshape(group_count, resident_adapters, MOST, hidden_cols)

    half = rows // 2
    w = down_projection_weight
    per_z = w.shape[1] // 4 // TILE
    h_a, h_b = hidden[:half], hidden[half:]
    iz, iy = lax.axis_index("z"), lax.axis_index("y")

    def z_block(k, first=0, count=per_z):
        return feature_tiles(h_a, w, (k * per_z + first) // 2, 1, count // 2, 2 * TILE)

    def y_block(k, first=0, count=per_z):
        return feature_tiles(h_b, w, k + first * per_z, per_z, count)

    def stage_one(block, i, axis):
        far = (i + 2) % 4
        hc = per_z // 2
        return _ring_stage(
            block(far, 0, hc), block(far, hc, hc), block((i + 1) % 4), block((i - 1) % 4), block(i),
            axis, False, 1,
        )

    partial_mix = jnp.einsum(
        "dlmf,lrf->dlmr", mine, adapter_down_maps, preferred_element_type=jnp.float32
    )

    red_a = reduce_scatter_axis(stage_one(z_block, iz, "z"), "y", 4)
    red_b = reduce_scatter_axis(stage_one(y_block, iy, "y"), "z", 4)
    base_rows = jnp.concatenate(
        [reduce_scatter_axis(red_a, "xl", 2, out_f32=True), reduce_scatter_axis(red_b, "xl", 2, out_f32=True)],
        axis=0,
    )

    mix = partial_mix
    for axis, n in (("xl", 2), ("y", 4), ("z", 4)):
        mix = all_reduce_axis(mix, axis, n)
    rank_mix = mix.astype(jnp.bfloat16)
    delta_mine = jnp.einsum(
        "dlmr,lrc->dlmc", rank_mix, adapter_up_maps, preferred_element_type=jnp.float32
    ).astype(jnp.bfloat16)
    feature_cols = delta_mine.shape[-1]
    delta_mine = delta_mine.reshape(group_count, per_owner, feature_cols)

    back = [delta_mine[0]]
    for d in range(1, group_count):
        perm = [(j, (j - d) % group_count) for j in range(group_count)]
        back.append(lax.ppermute(delta_mine[d], GROUP, perm))
    back = jnp.stack(back).reshape(group_count * per_owner, feature_cols)
    owner = slot_index // per_owner
    place = ((owner - g) % group_count) * per_owner + slot_index % per_owner
    delta_rows = back[place]

    total = residual.astype(jnp.float32) + base_rows + delta_rows.astype(jnp.float32)
    return total.astype(jnp.bfloat16)


def solution(mesh):
    fine = Mesh(mesh.devices.reshape(2, 2, 4, 4, 2), GROUP + TP)
    in_specs = (
        P(GROUP, TP),
        P(GROUP, TP),
        P(TP, None),
        P(GROUP, None, TP),
        P(GROUP, None, TP),
        P(GROUP, None),
    )
    out_specs = P(GROUP, TP)
    return jax.shard_map(
        per_device, mesh=fine, in_specs=in_specs, out_specs=out_specs, check_vma=False
    )
```

```python
import jax
import jax.numpy as jnp
from jax import lax
from jax.experimental import pallas as pl
from jax.experimental.pallas import tpu as pltpu
from jax.sharding import Mesh
from jax.sharding import PartitionSpec as P

MOST = 16
GROUP = ("xh", "c")
TP = ("z", "y", "xl")


def _pick(x, k, dim):
    return lax.dynamic_index_in_dim(x, k, dim, keepdims=False)


TILE = 512


def feature_tiles(h, w, base, stride, count):
    rows, depth = h.shape

    def kernel(base_ref, h_ref, w_ref, o_ref):
        o_ref[...] = jnp.dot(h_ref[...], w_ref[...], preferred_element_type=jnp.float32).astype(o_ref.dtype)

    return pl.pallas_call(
        kernel,
        out_shape=jax.ShapeDtypeStruct((rows, count * TILE), jnp.bfloat16),
        grid_spec=pltpu.PrefetchScalarGridSpec(
            num_scalar_prefetch=1,
            grid=(count,),
            in_specs=[
                pl.BlockSpec((rows, depth), lambda t, b: (0, 0)),
                pl.BlockSpec((depth, TILE), lambda t, b: (0, b[0] + t * stride)),
            ],
            out_specs=pl.BlockSpec((rows, TILE), lambda t, b: (0, t)),
        ),
        cost_estimate=pl.CostEstimate(
            flops=2 * rows * depth * TILE * count,
            bytes_accessed=2 * (rows * depth + depth * TILE * count + rows * TILE * count),
            transcendentals=0,
        ),
    )(jnp.reshape(base, (1,)).astype(jnp.int32), h, w)


def _ring_stage(far_a, far_b, nxt, prv, own, axis, out_f32, dim):
    f32 = jnp.float32
    n = 4
    fw = [(j, (j + 1) % n) for j in range(n)]
    bw = [(j, (j - 1) % n) for j in range(n)]
    h = far_a.shape[dim]
    got_a = lax.ppermute(far_a, axis, fw)
    got_b = lax.ppermute(far_b, axis, bw)
    lo = lambda x: lax.slice_in_dim(x, 0, h, axis=dim)
    hi = lambda x: lax.slice_in_dim(x, h, 2 * h, axis=dim)
    to_next = jnp.concatenate(
        [(lo(nxt).astype(f32) + got_a.astype(f32)).astype(jnp.bfloat16), hi(nxt)], axis=dim
    )
    to_prev = jnp.concatenate(
        [lo(prv), (hi(prv).astype(f32) + got_b.astype(f32)).astype(jnp.bfloat16)], axis=dim
    )
    from_prev = lax.ppermute(to_next, axis, fw)
    from_next = lax.ppermute(to_prev, axis, bw)
    total = from_prev.astype(f32) + from_next.astype(f32) + own.astype(f32)
    return total if out_f32 else total.astype(jnp.bfloat16)


def reduce_scatter_axis(x, axis, n, out_f32=False):
    i = lax.axis_index(axis)
    width = x.shape[1] // n
    pick = lambda k: lax.dynamic_slice_in_dim(x, k * width, width, axis=1)
    if n == 2:
        recv = lax.ppermute(pick(1 - i), axis, [(0, 1), (1, 0)])
        total = recv.astype(jnp.float32) + pick(i).astype(jnp.float32)
        return total if out_f32 else total.astype(jnp.bfloat16)
    far = pick((i + 2) % n)
    h = width // 2
    return _ring_stage(
        far[:, :h], far[:, h:], pick((i + 1) % n), pick((i - 1) % n), pick(i), axis, out_f32, 1
    )


def all_reduce_axis(x, axis, n):
    total = x
    sent = x.astype(jnp.bfloat16)
    for d in range(1, n):
        total = total + lax.ppermute(sent, axis, [(j, (j + d) % n) for j in range(n)]).astype(jnp.float32)
    return total


def per_device(
    hidden, residual, down_projection_weight, adapter_down_maps, adapter_up_maps, row_adapter_index
):
    group_count = 4
    rows, hidden_cols = hidden.shape
    resident_adapters = adapter_down_maps.shape[0]
    adapter_total = resident_adapters * group_count
    per_owner = resident_adapters * MOST
    g = lax.axis_index(GROUP)

    row_adapter = row_adapter_index[:, 0]
    one_hot = (row_adapter[:, None] == jnp.arange(adapter_total, dtype=jnp.int32)[None, :]).astype(
        jnp.int32
    )
    before = jnp.cumsum(one_hot, axis=0) - 1
    slot_rank = jnp.sum(one_hot * before, axis=1)
    slot_index = row_adapter * MOST + slot_rank
    parcels = jnp.zeros((adapter_total * MOST, hidden_cols), jnp.bfloat16).at[slot_index].set(hidden)
    parcels = parcels.reshape(group_count, per_owner, hidden_cols)

    shifted = [_pick(parcels, g, 0)]
    for d in range(1, group_count):
        perm = [(j, (j + d) % group_count) for j in range(group_count)]
        shifted.append(lax.ppermute(_pick(parcels, (g + d) % group_count, 0), GROUP, perm))
    mine = jnp.stack(shifted).reshape(group_count, resident_adapters, MOST, hidden_cols)

    half = rows // 2
    w = down_projection_weight
    per_z = w.shape[1] // 4 // TILE
    h_a, h_b = hidden[:half], hidden[half:]
    iz, iy = lax.axis_index("z"), lax.axis_index("y")

    def z_block(k, first=0, count=per_z):
        return feature_tiles(h_a, w, k * per_z + first, 1, count)

    def y_block(k, first=0, count=per_z):
        return feature_tiles(h_b, w, k + first * per_z, per_z, count)

    def stage_one(block, i, axis):
        far = (i + 2) % 4
        hc = per_z // 2
        return _ring_stage(
            block(far, 0, hc), block(far, hc, hc), block((i + 1) % 4), block((i - 1) % 4), block(i),
            axis, False, 1,
        )

    partial_mix = jnp.einsum(
        "dlmf,lrf->dlmr", mine, adapter_down_maps, preferred_element_type=jnp.float32
    )

    red_a = reduce_scatter_axis(stage_one(z_block, iz, "z"), "y", 4)
    red_b = reduce_scatter_axis(stage_one(y_block, iy, "y"), "z", 4)
    base_rows = jnp.concatenate(
        [reduce_scatter_axis(red_a, "xl", 2, out_f32=True), reduce_scatter_axis(red_b, "xl", 2, out_f32=True)],
        axis=0,
    )

    mix = partial_mix
    for axis, n in (("xl", 2), ("z", 4), ("y", 4)):
        mix = all_reduce_axis(mix, axis, n)
    rank_mix = mix.astype(jnp.bfloat16)
    delta_mine = jnp.einsum(
        "dlmr,lrc->dlmc", rank_mix, adapter_up_maps, preferred_element_type=jnp.float32
    ).astype(jnp.bfloat16)
    feature_cols = delta_mine.shape[-1]
    delta_mine = delta_mine.reshape(group_count, per_owner, feature_cols)

    back = [delta_mine[0]]
    for d in range(1, group_count):
        perm = [(j, (j - d) % group_count) for j in range(group_count)]
        back.append(lax.ppermute(delta_mine[d], GROUP, perm))
    back = jnp.stack(back).reshape(group_count * per_owner, feature_cols)
    owner = slot_index // per_owner
    place = ((owner - g) % group_count) * per_owner + slot_index % per_owner
    chooser = (place[:, None] == jnp.arange(back.shape[0], dtype=jnp.int32)[None, :]).astype(jnp.bfloat16)
    delta_rows = jnp.dot(chooser, back, preferred_element_type=jnp.float32)

    total = residual.astype(jnp.float32) + base_rows + delta_rows
    return total.astype(jnp.bfloat16)


def solution(mesh):
    fine = Mesh(mesh.devices.reshape(2, 2, 4, 4, 2), GROUP + TP)
    in_specs = (
        P(GROUP, TP),
        P(GROUP, TP),
        P(TP, None),
        P(GROUP, None, TP),
        P(GROUP, None, TP),
        P(GROUP, None),
    )
    out_specs = P(GROUP, TP)
    return jax.shard_map(
        per_device, mesh=fine, in_specs=in_specs, out_specs=out_specs, check_vma=False
    )
```

```python
import jax
import jax.numpy as jnp
from jax import lax
from jax.experimental import pallas as pl
from jax.experimental.pallas import tpu as pltpu
from jax.sharding import Mesh
from jax.sharding import PartitionSpec as P

MOST = 16
GROUP = ("xh", "c")
TP = ("z", "y", "xl")


def _pick(x, k, dim):
    return lax.dynamic_index_in_dim(x, k, dim, keepdims=False)


TILE = 512


def feature_tiles(h, w, base, stride, count):
    rows, depth = h.shape

    def kernel(base_ref, h_ref, w_ref, o_ref):
        o_ref[...] = jnp.dot(h_ref[...], w_ref[...], preferred_element_type=jnp.float32).astype(o_ref.dtype)

    return pl.pallas_call(
        kernel,
        out_shape=jax.ShapeDtypeStruct((rows, count * TILE), jnp.bfloat16),
        grid_spec=pltpu.PrefetchScalarGridSpec(
            num_scalar_prefetch=1,
            grid=(count,),
            in_specs=[
                pl.BlockSpec((rows, depth), lambda t, b: (0, 0)),
                pl.BlockSpec((depth, TILE), lambda t, b: (0, b[0] + t * stride)),
            ],
            out_specs=pl.BlockSpec((rows, TILE), lambda t, b: (0, t)),
        ),
        cost_estimate=pl.CostEstimate(
            flops=2 * rows * depth * TILE * count,
            bytes_accessed=2 * (rows * depth + depth * TILE * count + rows * TILE * count),
            transcendentals=0,
        ),
    )(jnp.reshape(base, (1,)).astype(jnp.int32), h, w)


def _ring_stage(far_a, far_b, nxt, prv, own, axis, out_f32, dim):
    f32 = jnp.float32
    n = 4
    fw = [(j, (j + 1) % n) for j in range(n)]
    bw = [(j, (j - 1) % n) for j in range(n)]
    h = far_a.shape[dim]
    got_a = lax.ppermute(far_a, axis, fw)
    got_b = lax.ppermute(far_b, axis, bw)
    lo = lambda x: lax.slice_in_dim(x, 0, h, axis=dim)
    hi = lambda x: lax.slice_in_dim(x, h, 2 * h, axis=dim)
    to_next = jnp.concatenate(
        [(lo(nxt).astype(f32) + got_a.astype(f32)).astype(jnp.bfloat16), hi(nxt)], axis=dim
    )
    to_prev = jnp.concatenate(
        [lo(prv), (hi(prv).astype(f32) + got_b.astype(f32)).astype(jnp.bfloat16)], axis=dim
    )
    from_prev = lax.ppermute(to_next, axis, fw)
    from_next = lax.ppermute(to_prev, axis, bw)
    total = from_prev.astype(f32) + from_next.astype(f32) + own.astype(f32)
    return total if out_f32 else total.astype(jnp.bfloat16)


def reduce_scatter_axis(x, axis, n, out_f32=False):
    i = lax.axis_index(axis)
    width = x.shape[1] // n
    pick = lambda k: lax.dynamic_slice_in_dim(x, k * width, width, axis=1)
    if n == 2:
        recv = lax.ppermute(pick(1 - i), axis, [(0, 1), (1, 0)])
        total = recv.astype(jnp.float32) + pick(i).astype(jnp.float32)
        return total if out_f32 else total.astype(jnp.bfloat16)
    far = pick((i + 2) % n)
    h = width // 2
    return _ring_stage(
        far[:, :h], far[:, h:], pick((i + 1) % n), pick((i - 1) % n), pick(i), axis, out_f32, 1
    )


def all_reduce_axis(x, axis, n):
    total = x
    sent = x.astype(jnp.bfloat16)
    for d in range(1, n):
        total = total + lax.ppermute(sent, axis, [(j, (j + d) % n) for j in range(n)]).astype(jnp.float32)
    return total


def per_device(
    hidden, residual, down_projection_weight, adapter_down_maps, adapter_up_maps, row_adapter_index
):
    group_count = 4
    rows, hidden_cols = hidden.shape
    resident_adapters = adapter_down_maps.shape[0]
    adapter_total = resident_adapters * group_count
    per_owner = resident_adapters * MOST
    g = lax.axis_index(GROUP)

    row_adapter = row_adapter_index[:, 0]
    one_hot = (row_adapter[:, None] == jnp.arange(adapter_total, dtype=jnp.int32)[None, :]).astype(
        jnp.int32
    )
    before = jnp.cumsum(one_hot, axis=0) - 1
    slot_rank = jnp.sum(one_hot * before, axis=1)
    slot_index = row_adapter * MOST + slot_rank
    parcels = jnp.zeros((adapter_total * MOST, hidden_cols), jnp.bfloat16).at[slot_index].set(hidden)
    parcels = parcels.reshape(group_count, per_owner, hidden_cols)

    shifted = [_pick(parcels, g, 0)]
    for d in range(1, group_count):
        perm = [(j, (j + d) % group_count) for j in range(group_count)]
        shifted.append(lax.ppermute(_pick(parcels, (g + d) % group_count, 0), GROUP, perm))
    mine = jnp.stack(shifted).reshape(group_count, resident_adapters, MOST, hidden_cols)

    half = rows // 2
    w = down_projection_weight
    per_z = w.shape[1] // 4 // TILE
    h_a, h_b = hidden[:half], hidden[half:]
    iz, iy = lax.axis_index("z"), lax.axis_index("y")

    def z_block(k, first=0, count=per_z):
        return feature_tiles(h_a, w, k * per_z + first, 1, count)

    def y_block(k, first=0, count=per_z):
        return feature_tiles(h_b, w, k + first * per_z, per_z, count)

    def stage_one(block, i, axis):
        far = (i + 2) % 4
        hc = per_z // 2
        return _ring_stage(
            block(far, 0, hc), block(far, hc, hc), block((i + 1) % 4), block((i - 1) % 4), block(i),
            axis, False, 1,
        )

    partial_mix = jnp.einsum(
        "dlmf,lrf->dlmr", mine, adapter_down_maps, preferred_element_type=jnp.float32
    )

    red_a = reduce_scatter_axis(stage_one(z_block, iz, "z"), "y", 4)
    red_b = reduce_scatter_axis(stage_one(y_block, iy, "y"), "z", 4)
    base_rows = jnp.concatenate(
        [reduce_scatter_axis(red_a, "xl", 2, out_f32=True), reduce_scatter_axis(red_b, "xl", 2, out_f32=True)],
        axis=0,
    )

    ix = lax.axis_index("xl")
    pair = [(0, 1), (1, 0)]
    halves = partial_mix.reshape(2, group_count // 2, *partial_mix.shape[1:])
    mix = _pick(halves, ix, 0) + lax.ppermute(
        _pick(halves, 1 - ix, 0).astype(jnp.bfloat16), "xl", pair
    ).astype(jnp.float32)
    for axis, n in (("z", 4), ("y", 4)):
        mix = all_reduce_axis(mix, axis, n)
    mine_half = mix.astype(jnp.bfloat16)
    other_half = lax.ppermute(mine_half, "xl", pair)
    both_halves = jnp.where(ix == 0, jnp.stack([mine_half, other_half]), jnp.stack([other_half, mine_half]))
    rank_mix = both_halves.reshape(partial_mix.shape)
    delta_mine = jnp.einsum(
        "dlmr,lrc->dlmc", rank_mix, adapter_up_maps, preferred_element_type=jnp.float32
    ).astype(jnp.bfloat16)
    feature_cols = delta_mine.shape[-1]
    delta_mine = delta_mine.reshape(group_count, per_owner, feature_cols)

    back = [delta_mine[0]]
    for d in range(1, group_count):
        perm = [(j, (j - d) % group_count) for j in range(group_count)]
        back.append(lax.ppermute(delta_mine[d], GROUP, perm))
    back = jnp.stack(back).reshape(group_count * per_owner, feature_cols)
    owner = slot_index // per_owner
    place = ((owner - g) % group_count) * per_owner + slot_index % per_owner
    chooser = (place[:, None] == jnp.arange(back.shape[0], dtype=jnp.int32)[None, :]).astype(jnp.bfloat16)
    delta_rows = jnp.dot(chooser, back, preferred_element_type=jnp.float32)

    total = residual.astype(jnp.float32) + base_rows + delta_rows
    return total.astype(jnp.bfloat16)


def solution(mesh):
    fine = Mesh(mesh.devices.reshape(2, 2, 4, 4, 2), GROUP + TP)
    in_specs = (
        P(GROUP, TP),
        P(GROUP, TP),
        P(TP, None),
        P(GROUP, None, TP),
        P(GROUP, None, TP),
        P(GROUP, None),
    )
    out_specs = P(GROUP, TP)
    return jax.shard_map(
        per_device, mesh=fine, in_specs=in_specs, out_specs=out_specs, check_vma=False
    )
```

```python
import jax
import jax.numpy as jnp
from jax import lax
from jax.experimental import pallas as pl
from jax.experimental.pallas import tpu as pltpu
from jax.sharding import Mesh
from jax.sharding import PartitionSpec as P

MOST = 16
GROUP = ("xh", "c")
TP = ("z", "y", "xl")


def _pick(x, k, dim):
    return lax.dynamic_index_in_dim(x, k, dim, keepdims=False)


TILE = 512


def feature_tiles(h, w, base, stride, count):
    rows, depth = h.shape

    def kernel(base_ref, h_ref, w_ref, o_ref):
        o_ref[...] = jnp.dot(h_ref[...], w_ref[...], preferred_element_type=jnp.float32).astype(o_ref.dtype)

    return pl.pallas_call(
        kernel,
        out_shape=jax.ShapeDtypeStruct((rows, count * TILE), jnp.bfloat16),
        grid_spec=pltpu.PrefetchScalarGridSpec(
            num_scalar_prefetch=1,
            grid=(count,),
            in_specs=[
                pl.BlockSpec((rows, depth), lambda t, b: (0, 0)),
                pl.BlockSpec((depth, TILE), lambda t, b: (0, b[0] + t * stride)),
            ],
            out_specs=pl.BlockSpec((rows, TILE), lambda t, b: (0, t)),
        ),
        cost_estimate=pl.CostEstimate(
            flops=2 * rows * depth * TILE * count,
            bytes_accessed=2 * (rows * depth + depth * TILE * count + rows * TILE * count),
            transcendentals=0,
        ),
    )(jnp.reshape(base, (1,)).astype(jnp.int32), h, w)


def _ring_stage(far_a, far_b, nxt, prv, own, axis, out_f32, dim):
    f32 = jnp.float32
    n = 4
    fw = [(j, (j + 1) % n) for j in range(n)]
    bw = [(j, (j - 1) % n) for j in range(n)]
    h = far_a.shape[dim]
    got_a = lax.ppermute(far_a, axis, fw)
    got_b = lax.ppermute(far_b, axis, bw)
    lo = lambda x: lax.slice_in_dim(x, 0, h, axis=dim)
    hi = lambda x: lax.slice_in_dim(x, h, 2 * h, axis=dim)
    to_next = jnp.concatenate(
        [(lo(nxt).astype(f32) + got_a.astype(f32)).astype(jnp.bfloat16), hi(nxt)], axis=dim
    )
    to_prev = jnp.concatenate(
        [lo(prv), (hi(prv).astype(f32) + got_b.astype(f32)).astype(jnp.bfloat16)], axis=dim
    )
    from_prev = lax.ppermute(to_next, axis, fw)
    from_next = lax.ppermute(to_prev, axis, bw)
    total = from_prev.astype(f32) + from_next.astype(f32) + own.astype(f32)
    return total if out_f32 else total.astype(jnp.bfloat16)


def reduce_scatter_axis(x, axis, n, out_f32=False):
    i = lax.axis_index(axis)
    width = x.shape[1] // n
    pick = lambda k: lax.dynamic_slice_in_dim(x, k * width, width, axis=1)
    if n == 2:
        recv = lax.ppermute(pick(1 - i), axis, [(0, 1), (1, 0)])
        total = recv.astype(jnp.float32) + pick(i).astype(jnp.float32)
        return total if out_f32 else total.astype(jnp.bfloat16)
    far = pick((i + 2) % n)
    h = width // 2
    return _ring_stage(
        far[:, :h], far[:, h:], pick((i + 1) % n), pick((i - 1) % n), pick(i), axis, out_f32, 1
    )


def all_reduce_axis(x, axis, n):
    total = x
    sent = x.astype(jnp.bfloat16)
    for d in range(1, n):
        total = total + lax.ppermute(sent, axis, [(j, (j + d) % n) for j in range(n)]).astype(jnp.float32)
    return total


def per_device(
    hidden, residual, down_projection_weight, adapter_down_maps, adapter_up_maps, row_adapter_index
):
    group_count = 4
    rows, hidden_cols = hidden.shape
    resident_adapters = adapter_down_maps.shape[0]
    adapter_total = resident_adapters * group_count
    per_owner = resident_adapters * MOST
    g = lax.axis_index(GROUP)

    row_adapter = row_adapter_index[:, 0]
    one_hot = (row_adapter[:, None] == jnp.arange(adapter_total, dtype=jnp.int32)[None, :]).astype(
        jnp.int32
    )
    before = jnp.cumsum(one_hot, axis=0) - 1
    slot_rank = jnp.sum(one_hot * before, axis=1)
    slot_index = row_adapter * MOST + slot_rank
    parcels = jnp.zeros((adapter_total * MOST, hidden_cols), jnp.bfloat16).at[slot_index].set(hidden)
    parcels = parcels.reshape(group_count, per_owner, hidden_cols)

    shifted = [_pick(parcels, g, 0)]
    for d in range(1, group_count):
        perm = [(j, (j + d) % group_count) for j in range(group_count)]
        shifted.append(lax.ppermute(_pick(parcels, (g + d) % group_count, 0), GROUP, perm))
    mine = jnp.stack(shifted).reshape(group_count, resident_adapters, MOST, hidden_cols)

    half = rows // 2
    w = down_projection_weight
    per_z = w.shape[1] // 4 // TILE
    h_a, h_b = hidden[:half], hidden[half:]
    iz, iy = lax.axis_index("z"), lax.axis_index("y")

    def z_block(k, first=0, count=per_z):
        return feature_tiles(h_a, w, k * per_z + first, 1, count)

    def y_block(k, first=0, count=per_z):
        return feature_tiles(h_b, w, k + first * per_z, per_z, count)

    def stage_one(block, i, axis):
        far = (i + 2) % 4
        hc = per_z // 2
        return _ring_stage(
            block(far, 0, hc), block(far, hc, hc), block((i + 1) % 4), block((i - 1) % 4), block(i),
            axis, False, 1,
        )

    partial_mix = jnp.einsum(
        "dlmf,lrf->dlmr", mine, adapter_down_maps, preferred_element_type=jnp.float32
    )

    red_a = reduce_scatter_axis(stage_one(z_block, iz, "z"), "y", 4)
    red_b = reduce_scatter_axis(stage_one(y_block, iy, "y"), "z", 4)
    base_rows = jnp.concatenate(
        [reduce_scatter_axis(red_a, "xl", 2, out_f32=True), reduce_scatter_axis(red_b, "xl", 2, out_f32=True)],
        axis=0,
    )

    ix = lax.axis_index("xl")
    pair = [(0, 1), (1, 0)]
    halves = partial_mix.reshape(2, group_count // 2, *partial_mix.shape[1:])
    mix = _pick(halves, ix, 0) + lax.ppermute(
        _pick(halves, 1 - ix, 0).astype(jnp.bfloat16), "xl", pair
    ).astype(jnp.float32)
    iz_ = lax.axis_index("z")
    quarters = mix.reshape(4, 128, -1).transpose(1, 0, 2).reshape(128, -1)
    part = reduce_scatter_axis(quarters.astype(jnp.bfloat16), "z", 4, out_f32=True)
    part = all_reduce_axis(part, "y", 4).astype(jnp.bfloat16)
    got = [part] + [
        lax.ppermute(part, "z", [(j, (j + d) % 4) for j in range(4)]) for d in range(1, 4)
    ]
    stacked = jnp.stack(got)
    gathered = jnp.stack([_pick(stacked, (iz_ - q) % 4, 0) for q in range(4)])
    mine_half = gathered.reshape(mix.shape)
    other_half = lax.ppermute(mine_half, "xl", pair)
    both_halves = jnp.where(ix == 0, jnp.stack([mine_half, other_half]), jnp.stack([other_half, mine_half]))
    rank_mix = both_halves.reshape(partial_mix.shape)
    delta_mine = jnp.einsum(
        "dlmr,lrc->dlmc", rank_mix, adapter_up_maps, preferred_element_type=jnp.float32
    ).astype(jnp.bfloat16)
    feature_cols = delta_mine.shape[-1]
    delta_mine = delta_mine.reshape(group_count, per_owner, feature_cols)

    back = [delta_mine[0]]
    for d in range(1, group_count):
        perm = [(j, (j - d) % group_count) for j in range(group_count)]
        back.append(lax.ppermute(delta_mine[d], GROUP, perm))
    back = jnp.stack(back).reshape(group_count * per_owner, feature_cols)
    owner = slot_index // per_owner
    place = ((owner - g) % group_count) * per_owner + slot_index % per_owner
    chooser = (place[:, None] == jnp.arange(back.shape[0], dtype=jnp.int32)[None, :]).astype(jnp.bfloat16)
    delta_rows = jnp.dot(chooser, back, preferred_element_type=jnp.float32)

    total = residual.astype(jnp.float32) + base_rows + delta_rows
    return total.astype(jnp.bfloat16)


def solution(mesh):
    fine = Mesh(mesh.devices.reshape(2, 2, 4, 4, 2), GROUP + TP)
    in_specs = (
        P(GROUP, TP),
        P(GROUP, TP),
        P(TP, None),
        P(GROUP, None, TP),
        P(GROUP, None, TP),
        P(GROUP, None),
    )
    out_specs = P(GROUP, TP)
    return jax.shard_map(
        per_device, mesh=fine, in_specs=in_specs, out_specs=out_specs, check_vma=False
    )
```
